32 devices in a mesh: rows: 16 (over z, y, x), cov: 2 (over core).
Axes of the slice: x: 2, y: 2, z: 4, core: 2. Of those that a mesh axis runs over, the one named last changes fastest.
Arguments:
- design: bfloat16 [49152, 1024], P('rows', 'cov')
- tract_id: int32 [49152], P('rows'), may hold values from 0 to 21247, as said below
- outcome: int32 [49152], P('rows'), may hold values 0 or 1
- omega: float32 [49152], P('rows'), may hold values from 0.05 to 0.5
- effects_old: float32 [21248], P('rows'), may hold values from -6 to 6
- normal_coef: float32 [1024], P('cov'), may hold values from -6 to 6
- normal_tract: float32 [21248], P('rows'), may hold values from -6 to 6
Outputs:
- beta: float32 [1024], P('cov')
- effects: float32 [21248], P('rows')
The draws below stay inside these ranges and needn't reach their ends.
Inputs may be any that keep to these rules, and one draw needn't show every extreme that they name: `tract_id`: A record on the device with index d along rows names a tract from (d - 1) * 1328 to (d + 2) * 1328 - 1, and also from 0 at d = 0 and up to 21247 at the last index; every device other than the first and last names both ends of its range. Some tracts hold many records and some none.
All inputs are finite; a program needn't handle non-finite values. No bound on the sum of `outcome` on one device may be relied on, other than what follows from the above.
Results may differ from the reference program's by a relative error of at most 0.0023.
Values may be sent and summed in bfloat16 or wider, within the bound.
No kernel may reach another device: no remote copies, remote signals or barrier semaphores. Data moves between devices by JAX's collectives and lax.ppermute only.
A program may use at most 128 MiB of HBM per device.

```python
import math
import jax
import jax.numpy as jnp
from jax import lax

P_SIZE = 1024
R_DEV = 3072
TRACT_DEV = 1328
ROWS = 49152
NT = 21248
N_ROWS = 16


def draw_design(key, part):
    first, second, third, fourth = jax.random.split(key, 4)
    factor = 2.0 / jnp.sqrt(0.2 * ROWS)
    signs = jnp.where(jax.random.bernoulli(third, 0.5, (8, P_SIZE)), 1.0, -1.0)
    loading = signs * jax.random.uniform(fourth, (8, P_SIZE), jnp.float32, 0.6, 1.4)
    independent = jax.random.normal(first, (ROWS, P_SIZE), jnp.float32)
    shared = jax.random.normal(second, (ROWS, 8), jnp.float32)
    values = independent
    for level in range(8):
        values = values + 0.25 * shared[:, level:level + 1] * loading[level][None, :]
    return (factor * values).astype(jnp.bfloat16)


def draw_tract_id(key, part):
    first, second, third = jax.random.split(key, 3)
    places = jnp.arange(ROWS, dtype=jnp.int32)
    owner = places // R_DEV
    within = places % R_DEV
    span = 3 * TRACT_DEV
    drawn = jax.random.randint(first, (ROWS,), 0, span)
    heavy = jax.random.randint(second, (ROWS,), 0, max(span // 48, 1)) * 48
    picker = jax.random.randint(third, (ROWS,), 0, 2)
    offset = jnp.where(picker == 1, heavy, drawn)
    offset = jnp.where(within == 0, 0, offset)
    offset = jnp.where(within == 1, span - 1, offset)
    tract = (owner - 1) * TRACT_DEV + offset
    tract = jnp.where(tract < 0, tract + TRACT_DEV, tract)
    tract = jnp.where(tract >= NT, tract - TRACT_DEV, tract)
    return tract.astype(jnp.int32)


def place_ends(values, rng, smallest, high):
    longest = values.shape.index(max(values.shape))
    spots = []
    for shift in (0, 1):
        where = [jax.random.randint(jax.random.fold_in(rng, axis), (), 0, length) for axis, length in enumerate(values.shape)]
        where[longest] = (where[longest] + shift) % values.shape[longest]
        spots.append(tuple(where))
    return values.at[spots[0]].set(smallest).at[spots[1]].set(high)


def levels(stream_key, extent, pieces, smallest, high):
    factor_of = 1.0
    for position, shards_of in pieces:
        draws = jax.random.uniform(jax.random.fold_in(jax.random.fold_in(stream_key, 6), position), (shards_of,), jnp.float32, smallest / len(pieces), high / len(pieces))
        factor_of = factor_of * jnp.repeat(jnp.exp(draws), extent[position] // shards_of).reshape((-1,) + (1,) * (len(extent) - 1 - position))
    return factor_of


def noise(stream_key, dims, width, limit, shards=(), kind=jnp.bfloat16):
    array = jax.random.normal(stream_key, dims, jnp.float32) * width
    if len(shards) > 0:
        array = levels(stream_key, dims, shards, -0.22, 0.18) * array
    return jnp.clip(array, min=-limit, max=limit).astype(kind)


def setup_inputs(seed: int = 0) -> dict:
    arg_keys = jax.random.split(jax.random.key(seed), 8)
    return {
        "design": draw_design(jax.random.fold_in(arg_keys[7], 71), 0),
        "tract_id": draw_tract_id(jax.random.fold_in(arg_keys[7], 71), 0),
        "outcome": place_ends((jax.random.randint(arg_keys[2], (ROWS,), 0, 2) < 1).astype(jnp.int32), jax.random.fold_in(arg_keys[2], 1), 0, 1),
        "omega": jnp.clip(jnp.exp(math.log(0.5) - 2.3025851 * jax.random.uniform(arg_keys[3], (ROWS,), jnp.float32) ** levels(arg_keys[3], (ROWS,), ((0, 16),), -0.2, 0.2)), 0.05, 0.5),
        "effects_old": noise(arg_keys[4], (NT,), 1.0, 6.0, ((0, 16),), jnp.float32),
        "normal_coef": noise(arg_keys[5], (P_SIZE,), 1.0, 6.0, ((0, 2),), jnp.float32),
        "normal_tract": noise(arg_keys[6], (NT,), 1.0, 6.0, ((0, 16),), jnp.float32),
    }


prior_precision = 1.0
tract_precision = 1.0

def reference(design, tract_id, outcome, omega, effects_old, normal_coef, normal_tract):
    kappa = outcome.astype(jnp.float32) - 0.5
    resid = (kappa - omega * effects_old[tract_id]).astype(jnp.bfloat16)
    blocks_x = design.reshape(N_ROWS, R_DEV, P_SIZE)
    blocks_w = omega.reshape(N_ROWS, R_DEV)
    blocks_r = resid.reshape(N_ROWS, R_DEV)

    def accumulate(carry, block):
        rows_x, rows_w, rows_r = block
        weighted = (rows_w[:, None] * rows_x).astype(jnp.bfloat16)
        gram = carry[0] + jnp.dot(rows_x.T.astype(jnp.float32), weighted.astype(jnp.float32), preferred_element_type=jnp.float32)
        rhs = carry[1] + jnp.dot(rows_r.astype(jnp.float32), rows_x.astype(jnp.float32), preferred_element_type=jnp.float32)
        return ((gram, rhs), None)
    start = (jnp.zeros((P_SIZE, P_SIZE), jnp.float32), jnp.zeros((P_SIZE,), jnp.float32))
    (gram, rhs), _ = lax.scan(accumulate, start, (blocks_x, blocks_w, blocks_r))
    precision = 0.5 * (gram + gram.T) + prior_precision * jnp.eye(P_SIZE, dtype=jnp.float32)
    lower = jnp.linalg.cholesky(precision)
    inner = jax.scipy.linalg.solve_triangular(lower, rhs, lower=True) + normal_coef
    beta = jax.scipy.linalg.solve_triangular(lower, inner, trans=1, lower=True)
    beta_b = beta.astype(jnp.bfloat16)
    eta = jnp.dot(design.astype(jnp.float32), beta_b.astype(jnp.float32), preferred_element_type=jnp.float32)
    contrib = kappa - omega * eta
    prec = tract_precision + jax.ops.segment_sum(omega, tract_id, num_segments=NT)
    num = jax.ops.segment_sum(contrib, tract_id, num_segments=NT)
    effects = num / prec + normal_tract / jnp.sqrt(prec)
    return (beta, effects)
```

```python
import jax
import jax.numpy as jnp
from jax import lax
from jax.sharding import PartitionSpec as P

prior_precision = 1.0
tract_precision = 1.0
BLOCK = 128
HIGH = lax.Precision.HIGHEST


def extended(block, sides, width):
    for axis, dim in sides:
        count = lax.axis_size(axis)
        forward = [(i, i + 1) for i in range(count - 1)]
        backward = [(target, source) for source, target in forward]
        low = lax.ppermute(
            lax.slice_in_dim(block, block.shape[dim] - width, None, axis=dim), axis, forward
        )
        high = lax.ppermute(lax.slice_in_dim(block, 0, width, axis=dim), axis, backward)
        block = jnp.concatenate([low, block, high], axis=dim)
    return block


def from_behind(block, axis, distance):
    devices = range(lax.axis_size(axis))
    route = [(i - distance, i) for i in devices if i - distance in devices]
    return lax.ppermute(block, axis, route)


def contract_rows(left, right):
    return lax.dot_general(
        left, right, (((0,), (0,)), ((), ())), preferred_element_type=jnp.float32
    )


def mm(a, b):
    return jnp.dot(a, b, precision=HIGH, preferred_element_type=jnp.float32)


def factor(precision):
    order = precision.shape[0]
    eye = jnp.eye(BLOCK, dtype=jnp.float32)
    trailing = precision
    inverses, panels = [], []
    for k in range(order // BLOCK):
        diag = lax.linalg.cholesky(trailing[:BLOCK, :BLOCK], symmetrize_input=False)
        inverse = lax.linalg.triangular_solve(diag, eye, left_side=True, lower=True)
        inverses.append(inverse)
        if trailing.shape[0] > BLOCK:
            panel = mm(trailing[BLOCK:, :BLOCK], inverse.T)
            panels.append(panel)
            trailing = trailing[BLOCK:, BLOCK:] - mm(panel, panel.T)
    return inverses, panels


def draw(inverses, panels, rhs, noise):
    count = len(inverses)
    rest = rhs
    inner = []
    for k in range(count):
        part = mm(inverses[k], rest[:BLOCK])
        inner.append(part + noise[k * BLOCK : (k + 1) * BLOCK])
        if k < count - 1:
            rest = rest[BLOCK:] - mm(panels[k], part)
    solved = []
    below = None
    for k in reversed(range(count)):
        value = inner[k]
        if below is not None:
            value = value - mm(panels[k].T, below)
        part = mm(inverses[k].T, value)
        solved.insert(0, part)
        below = part if below is None else jnp.concatenate([part, below])
    return jnp.concatenate(solved)


def local(design, tract_id, outcome, omega, effects_old, normal_coef, normal_tract):
    columns = design.shape[1]
    tract_dev = effects_old.shape[0]
    kappa = outcome.astype(jnp.float32) - 0.5
    window = extended(effects_old, (("rows", 0),), tract_dev)
    local_id = tract_id - (lax.axis_index("rows") - 1) * tract_dev
    effect_row = jnp.take(window, local_id)
    resid = (kappa - omega * effect_row).astype(jnp.bfloat16)
    offset = lax.axis_index("cov") * columns
    weighted = (omega[:, None] * design).astype(jnp.bfloat16)
    gram_block = contract_rows(lax.all_gather(design, "cov", axis=1, tiled=True), weighted)
    rhs_block = contract_rows(resid, design)
    pad = jnp.zeros((7, columns), jnp.float32)
    stacked = jnp.concatenate([gram_block, rhs_block[None, :], normal_coef[None, :], pad])
    order = gram_block.shape[0]
    summed = jnp.concatenate([lax.psum(stacked[: order + 1], "rows"), stacked[order + 1 :]])
    full = lax.all_gather(summed, "cov", axis=1, tiled=True)
    gram, rhs, noise = full[:order], full[order], full[order + 1]
    precision = 0.5 * (gram + gram.T) + prior_precision * jnp.eye(order, dtype=jnp.float32)
    inverses, panels = factor(precision)
    beta = draw(inverses, panels, rhs, noise)
    beta_b = beta.astype(jnp.bfloat16)
    beta_own = lax.dynamic_slice_in_dim(beta, offset, columns)
    own_coef = lax.dynamic_slice_in_dim(beta_b, offset, columns)
    partial_eta = jnp.dot(design, own_coef, preferred_element_type=jnp.float32)
    eta = lax.psum(partial_eta, "cov")
    contrib = kappa - omega * eta
    weight_sums = jax.ops.segment_sum(omega, local_id, num_segments=3 * tract_dev)
    resid_sums = jax.ops.segment_sum(contrib, local_id, num_segments=3 * tract_dev)
    from_above = from_behind((weight_sums[:tract_dev], resid_sums[:tract_dev]), "rows", -1)
    from_below = from_behind((weight_sums[2 * tract_dev :], resid_sums[2 * tract_dev :]), "rows", 1)
    weight_total = weight_sums[tract_dev : 2 * tract_dev] + from_above[0] + from_below[0]
    resid_total = resid_sums[tract_dev : 2 * tract_dev] + from_above[1] + from_below[1]
    prec = tract_precision + weight_total
    effects = resid_total / prec + normal_tract * lax.rsqrt(prec)
    return (beta_own, effects)


def solution(mesh):
    placed = (P("rows", "cov"), P("rows"), P("rows"), P("rows"), P("rows"), P("cov"), P("rows"))
    return jax.shard_map(
        local, mesh=mesh, in_specs=placed, out_specs=(P("cov"), P("rows")), check_vma=False
    )
```

```python
import jax
import jax.numpy as jnp
from jax import lax
from jax.experimental import pallas as pl
from jax.experimental.pallas import tpu as pltpu
from jax.sharding import PartitionSpec as P

prior_precision = 1.0
tract_precision = 1.0
BLOCK = 128
HIGH = lax.Precision.HIGHEST


def extended(block, sides, width):
    for axis, dim in sides:
        count = lax.axis_size(axis)
        forward = [(i, i + 1) for i in range(count - 1)]
        backward = [(target, source) for source, target in forward]
        low = lax.ppermute(
            lax.slice_in_dim(block, block.shape[dim] - width, None, axis=dim), axis, forward
        )
        high = lax.ppermute(lax.slice_in_dim(block, 0, width, axis=dim), axis, backward)
        block = jnp.concatenate([low, block, high], axis=dim)
    return block


def from_behind(block, axis, distance):
    devices = range(lax.axis_size(axis))
    route = [(i - distance, i) for i in devices if i - distance in devices]
    return lax.ppermute(block, axis, route)


def contract_rows(left, right):
    return lax.dot_general(
        left, right, (((0,), (0,)), ((), ())), preferred_element_type=jnp.float32
    )


def mm(a, b):
    return jnp.dot(a, b, precision=HIGH, preferred_element_type=jnp.float32)


def inverse_kernel(a_ref, inv_ref, work):
    size = a_ref.shape[0]
    work[...] = a_ref[...]
    rows = lax.broadcasted_iota(jnp.int32, (size, size), 0)
    lanes = lax.broadcasted_iota(jnp.int32, (size, size), 1)
    inv_ref[...] = jnp.where(rows == lanes, 1.0, 0.0).astype(jnp.float32)
    lane = lax.broadcasted_iota(jnp.int32, (1, size), 1)
    sub = lax.broadcasted_iota(jnp.int32, (size, 1), 0)

    def step(k, carry):
        row = work[pl.ds(k, 1), :]
        pivot = jnp.sum(jnp.where(lane == k, row, 0.0), axis=1, keepdims=True)
        scale = lax.rsqrt(pivot)
        whole = work[...]
        column = jnp.sum(jnp.where(lanes == k, whole, 0.0), axis=1, keepdims=True)
        below = jnp.where(sub > k, column * scale, 0.0)
        tail = jnp.where(lane > k, row * scale, 0.0)
        work[...] = whole - below * tail
        lead = inv_ref[pl.ds(k, 1), :] * scale
        current = inv_ref[...]
        inv_ref[...] = jnp.where(rows == k, lead, current - below * lead)
        return carry

    lax.fori_loop(0, size, step, 0)


def block_inverse(block):
    size = block.shape[0]
    return pl.pallas_call(
        inverse_kernel,
        out_shape=jax.ShapeDtypeStruct((size, size), jnp.float32),
        in_specs=[pl.BlockSpec(memory_space=pltpu.VMEM)],
        out_specs=pl.BlockSpec(memory_space=pltpu.VMEM),
        scratch_shapes=[pltpu.VMEM((size, size), jnp.float32)],
        cost_estimate=pl.CostEstimate(flops=4 * size ** 3, bytes_accessed=8 * size * size, transcendentals=size),
    )(block)


def factor(precision, rhs):
    order = precision.shape[0]
    extra = jnp.zeros((8, order), jnp.float32).at[0].set(rhs)
    trailing = jnp.concatenate([precision, extra])
    inverses, panels, forward = [], [], []
    for k in range(order // BLOCK):
        inverse = block_inverse(trailing[:BLOCK, :BLOCK])
        inverses.append(inverse)
        full = mm(trailing[BLOCK:, :BLOCK], inverse.T)
        forward.append(full[-8])
        panel = full[:-8]
        if panel.shape[0]:
            panels.append(panel)
            trailing = trailing[BLOCK:, BLOCK:] - mm(full, panel.T)
    return inverses, panels, forward


def backward(inverses, panels, forward, noise):
    count = len(inverses)
    solved = []
    below = None
    for k in reversed(range(count)):
        value = forward[k] + noise[k * BLOCK : (k + 1) * BLOCK]
        if below is not None:
            value = value - mm(panels[k].T, below)
        part = mm(inverses[k].T, value)
        solved.insert(0, part)
        below = part if below is None else jnp.concatenate([part, below])
    return jnp.concatenate(solved)


def pair_gather(block, axis, dim):
    if lax.axis_size(axis) != 2:
        return lax.all_gather(block, axis, axis=dim, tiled=True)
    other = lax.ppermute(block, axis, [(0, 1), (1, 0)])
    first = lax.axis_index(axis) == 0
    return jnp.concatenate(
        [jnp.where(first, block, other), jnp.where(first, other, block)], axis=dim
    )


def pair_sum(block, axis):
    if lax.axis_size(axis) != 2:
        return lax.psum(block, axis)
    return block + lax.ppermute(block, axis, [(0, 1), (1, 0)])


def halving_sum(data, axis, late):
    count = lax.axis_size(axis)
    index = lax.axis_index(axis)
    bits = [1 << b for b in range(count.bit_length() - 1)]
    for bit in bits:
        route = [(i, i ^ bit) for i in range(count)]
        half = data.shape[0] // 2
        upper = (index & bit) != 0
        send = jnp.where(upper, data[:half], data[half:])
        keep = jnp.where(upper, data[half:], data[:half])
        data = keep + lax.ppermute(send, axis, route)
    data = jnp.concatenate([data, late])
    for bit in reversed(bits):
        route = [(i, i ^ bit) for i in range(count)]
        upper = (index & bit) != 0
        other = lax.ppermute(data, axis, route)
        data = jnp.concatenate(
            [jnp.where(upper, other, data), jnp.where(upper, data, other)]
        )
    return data.reshape(count, -1, data.shape[-1])


def local(design, tract_id, outcome, omega, effects_old, normal_coef, normal_tract):
    columns = design.shape[1]
    tract_dev = effects_old.shape[0]
    kappa = outcome.astype(jnp.float32) - 0.5
    window = extended(effects_old, (("rows", 0),), tract_dev)
    local_id = tract_id - (lax.axis_index("rows") - 1) * tract_dev
    effect_row = jnp.take(window, local_id)
    resid = (kappa - omega * effect_row).astype(jnp.bfloat16)
    core = lax.axis_index("cov")
    offset = core * columns
    half = columns // 2
    weighted = (omega[:, None] * design).astype(jnp.bfloat16)
    whole = pair_gather(design, "cov", 1)
    whole_w = (omega[:, None] * whole).astype(jnp.bfloat16)
    own_gram = contract_rows(design, weighted)
    own_sym = own_gram + own_gram.T
    first, second = whole[:, :columns], whole[:, columns:]
    first_w, second_w = whole_w[:, :columns], whole_w[:, columns:]
    cols = lax.dynamic_slice_in_dim(first, core * half, half, axis=1)
    cols_w = lax.dynamic_slice_in_dim(first_w, core * half, half, axis=1)
    cross = contract_rows(second, cols_w) + contract_rows(cols, second_w).T
    rhs_block = contract_rows(resid, design)
    weight_sums = jax.ops.segment_sum(omega, local_id, num_segments=3 * tract_dev)
    packed = jnp.concatenate([own_sym, cross], axis=1).reshape(-1, BLOCK)
    packed_rows = packed.shape[0]
    extra = columns // BLOCK
    count = lax.axis_size("rows")
    unit = 8 * count
    total = -(-packed_rows // unit) * unit
    if total > packed_rows:
        packed = jnp.concatenate([packed, jnp.zeros((total - packed_rows, BLOCK), jnp.float32)])
    late_rows = -(-extra // 8) * 8
    late = jnp.concatenate(
        [rhs_block.reshape(-1, BLOCK), jnp.zeros((late_rows - extra, BLOCK), jnp.float32)]
    ) + 0.0 * weight_sums[0]
    gathered = halving_sum(packed, "rows", late)
    chunk = total // count
    summed = gathered[:, :chunk].reshape(total, BLOCK)
    rhs_own = jnp.sum(gathered[:, chunk : chunk + extra], axis=0)
    tail = jnp.concatenate([rhs_own, normal_coef.reshape(-1, BLOCK)])
    both = pair_gather(jnp.concatenate([summed[:packed_rows], tail])[None], "cov", 0)
    rhs = both[:, packed_rows : packed_rows + extra].reshape(-1)
    noise = both[:, packed_rows + extra :].reshape(-1)
    blocks = both[:, :packed_rows].reshape(2, columns, columns + half)
    order = 2 * columns
    sym = jnp.concatenate(
        [
            jnp.concatenate([blocks[0, :, :columns], jnp.zeros((columns, columns), jnp.float32)], axis=1),
            jnp.concatenate([blocks[0, :, columns:], blocks[1, :, columns:], blocks[1, :, :columns]], axis=1),
        ]
    )
    precision = 0.5 * sym + prior_precision * jnp.eye(order, dtype=jnp.float32)
    inverses, panels, forward = factor(precision, rhs)
    beta = backward(inverses, panels, forward, noise)
    beta_b = beta.astype(jnp.bfloat16)
    beta_own = lax.dynamic_slice_in_dim(beta, offset, columns)
    own_coef = lax.dynamic_slice_in_dim(beta_b, offset, columns)
    partial_eta = jnp.dot(design, own_coef, preferred_element_type=jnp.float32)
    eta = pair_sum(partial_eta, "cov")
    contrib = kappa - omega * eta
    resid_sums = jax.ops.segment_sum(contrib, local_id, num_segments=3 * tract_dev)
    from_above = from_behind((weight_sums[:tract_dev], resid_sums[:tract_dev]), "rows", -1)
    from_below = from_behind((weight_sums[2 * tract_dev :], resid_sums[2 * tract_dev :]), "rows", 1)
    weight_total = weight_sums[tract_dev : 2 * tract_dev] + from_above[0] + from_below[0]
    resid_total = resid_sums[tract_dev : 2 * tract_dev] + from_above[1] + from_below[1]
    prec = tract_precision + weight_total
    effects = resid_total / prec + normal_tract * lax.rsqrt(prec)
    return (beta_own, effects)


def solution(mesh):
    placed = (P("rows", "cov"), P("rows"), P("rows"), P("rows"), P("rows"), P("cov"), P("rows"))
    return jax.shard_map(
        local, mesh=mesh, in_specs=placed, out_specs=(P("cov"), P("rows")), check_vma=False
    )
```

```python
import jax
import jax.numpy as jnp
from jax import lax
from jax.experimental import pallas as pl
from jax.experimental.pallas import tpu as pltpu
from jax.sharding import PartitionSpec as P

prior_precision = 1.0
tract_precision = 1.0
BLOCK = 128
HIGH = lax.Precision.HIGHEST


def extended(block, sides, width):
    for axis, dim in sides:
        count = lax.axis_size(axis)
        forward = [(i, i + 1) for i in range(count - 1)]
        backward = [(target, source) for source, target in forward]
        low = lax.ppermute(
            lax.slice_in_dim(block, block.shape[dim] - width, None, axis=dim), axis, forward
        )
        high = lax.ppermute(lax.slice_in_dim(block, 0, width, axis=dim), axis, backward)
        block = jnp.concatenate([low, block, high], axis=dim)
    return block


def from_behind(block, axis, distance):
    devices = range(lax.axis_size(axis))
    route = [(i - distance, i) for i in devices if i - distance in devices]
    return lax.ppermute(block, axis, route)


def contract_rows(left, right):
    return lax.dot_general(
        left, right, (((0,), (0,)), ((), ())), preferred_element_type=jnp.float32
    )


def mm(a, b):
    return jnp.dot(a, b, precision=HIGH, preferred_element_type=jnp.float32)


def inverse_kernel(a_ref, inv_ref, work):
    size = a_ref.shape[0]
    work[...] = a_ref[...]
    rows = lax.broadcasted_iota(jnp.int32, (size, size), 0)
    lanes = lax.broadcasted_iota(jnp.int32, (size, size), 1)
    inv_ref[...] = jnp.where(rows == lanes, 1.0, 0.0).astype(jnp.float32)
    lane = lax.broadcasted_iota(jnp.int32, (1, size), 1)
    sub = lax.broadcasted_iota(jnp.int32, (size, 1), 0)

    def step(k, carry):
        row = work[pl.ds(k, 1), :]
        pivot = jnp.sum(jnp.where(lane == k, row, 0.0), axis=1, keepdims=True)
        scale = lax.rsqrt(pivot)
        whole = work[...]
        column = jnp.sum(jnp.where(lanes == k, whole, 0.0), axis=1, keepdims=True)
        below = jnp.where(sub > k, column * scale, 0.0)
        tail = jnp.where(lane > k, row * scale, 0.0)
        work[...] = whole - below * tail
        lead = inv_ref[pl.ds(k, 1), :] * scale
        current = inv_ref[...]
        inv_ref[...] = jnp.where(rows == k, lead, current - below * lead)
        return carry

    lax.fori_loop(0, size, step, 0)


def block_inverse(block):
    size = block.shape[0]
    return pl.pallas_call(
        inverse_kernel,
        out_shape=jax.ShapeDtypeStruct((size, size), jnp.float32),
        in_specs=[pl.BlockSpec(memory_space=pltpu.VMEM)],
        out_specs=pl.BlockSpec(memory_space=pltpu.VMEM),
        scratch_shapes=[pltpu.VMEM((size, size), jnp.float32)],
        cost_estimate=pl.CostEstimate(flops=4 * size ** 3, bytes_accessed=8 * size * size, transcendentals=size),
    )(block)


def factor(precision, rhs):
    order = precision.shape[0]
    extra = jnp.zeros((8, order), jnp.float32).at[0].set(rhs)
    trailing = jnp.concatenate([precision, extra])
    inverses, panels, forward = [], [], []
    for k in range(order // BLOCK):
        inverse = block_inverse(trailing[:BLOCK, :BLOCK])
        inverses.append(inverse)
        full = mm(trailing[BLOCK:, :BLOCK], inverse.T)
        forward.append(full[-8])
        panel = full[:-8]
        if panel.shape[0]:
            panels.append(panel)
            trailing = trailing[BLOCK:, BLOCK:] - mm(full, panel.T)
    return inverses, panels, forward


def backward(inverses, panels, forward, noise):
    count = len(inverses)
    solved = []
    below = None
    for k in reversed(range(count)):
        value = forward[k] + noise[k * BLOCK : (k + 1) * BLOCK]
        if below is not None:
            value = value - mm(panels[k].T, below)
        part = mm(inverses[k].T, value)
        solved.insert(0, part)
        below = part if below is None else jnp.concatenate([part, below])
    return jnp.concatenate(solved)


def pair_gather(block, axis, dim):
    if lax.axis_size(axis) != 2:
        return lax.all_gather(block, axis, axis=dim, tiled=True)
    other = lax.ppermute(block, axis, [(0, 1), (1, 0)])
    first = lax.axis_index(axis) == 0
    return jnp.concatenate(
        [jnp.where(first, block, other), jnp.where(first, other, block)], axis=dim
    )


def pair_sum(block, axis):
    if lax.axis_size(axis) != 2:
        return lax.psum(block, axis)
    return block + lax.ppermute(block, axis, [(0, 1), (1, 0)])


def halving_sum(data, axis, late):
    count = lax.axis_size(axis)
    index = lax.axis_index(axis)
    bits = [1 << b for b in range(count.bit_length() - 1)]
    for bit in bits:
        route = [(i, i ^ bit) for i in range(count)]
        half = data.shape[0] // 2
        upper = (index & bit) != 0
        send = jnp.where(upper, data[:half], data[half:])
        keep = jnp.where(upper, data[half:], data[:half])
        data = keep + lax.ppermute(send, axis, route)
    data = jnp.concatenate([data, late])
    for bit in reversed(bits):
        route = [(i, i ^ bit) for i in range(count)]
        upper = (index & bit) != 0
        other = lax.ppermute(data, axis, route)
        data = jnp.concatenate(
            [jnp.where(upper, other, data), jnp.where(upper, data, other)]
        )
    return data.reshape(count, -1, data.shape[-1])


def one_hot(ids, size):
    return (ids[:, None] == lax.broadcasted_iota(jnp.int32, (1, size), 1)).astype(jnp.bfloat16)


def split_parts(values):
    high = values.astype(jnp.bfloat16)
    rest = values - high.astype(jnp.float32)
    middle = rest.astype(jnp.bfloat16)
    low = (rest - middle.astype(jnp.float32)).astype(jnp.bfloat16)
    return jnp.stack([high, middle, low], axis=1)


def take_rows(table, ids):
    parts = jnp.dot(one_hot(ids, table.shape[0]), split_parts(table), preferred_element_type=jnp.float32)
    return parts[:, 0] + (parts[:, 1] + parts[:, 2])


def segment_total(values, ids, size):
    parts = contract_rows(one_hot(ids, size), split_parts(values))
    return parts[:, 0] + (parts[:, 1] + parts[:, 2])


def local(design, tract_id, outcome, omega, effects_old, normal_coef, normal_tract):
    columns = design.shape[1]
    tract_dev = effects_old.shape[0]
    kappa = outcome.astype(jnp.float32) - 0.5
    window = extended(effects_old, (("rows", 0),), tract_dev)
    local_id = tract_id - (lax.axis_index("rows") - 1) * tract_dev
    effect_row = take_rows(window, local_id)
    resid = (kappa - omega * effect_row).astype(jnp.bfloat16)
    core = lax.axis_index("cov")
    offset = core * columns
    half = columns // 2
    weighted = (omega[:, None] * design).astype(jnp.bfloat16)
    whole = pair_gather(design, "cov", 1)
    whole_w = (omega[:, None] * whole).astype(jnp.bfloat16)
    own_gram = contract_rows(design, weighted)
    own_sym = own_gram + own_gram.T
    first, second = whole[:, :columns], whole[:, columns:]
    first_w, second_w = whole_w[:, :columns], whole_w[:, columns:]
    cols = lax.dynamic_slice_in_dim(first, core * half, half, axis=1)
    cols_w = lax.dynamic_slice_in_dim(first_w, core * half, half, axis=1)
    cross = contract_rows(second, cols_w) + contract_rows(cols, second_w).T
    rhs_block = contract_rows(resid, design)
    weight_sums = segment_total(omega, local_id, 3 * tract_dev)
    packed = jnp.concatenate([own_sym, cross], axis=1).reshape(-1, BLOCK)
    packed_rows = packed.shape[0]
    extra = columns // BLOCK
    count = lax.axis_size("rows")
    unit = 8 * count
    total = -(-packed_rows // unit) * unit
    if total > packed_rows:
        packed = jnp.concatenate([packed, jnp.zeros((total - packed_rows, BLOCK), jnp.float32)])
    late_rows = -(-extra // 8) * 8
    late = jnp.concatenate(
        [rhs_block.reshape(-1, BLOCK), jnp.zeros((late_rows - extra, BLOCK), jnp.float32)]
    ) + 0.0 * weight_sums[0]
    gathered = halving_sum(packed, "rows", late)
    chunk = total // count
    summed = gathered[:, :chunk].reshape(total, BLOCK)
    rhs_own = jnp.sum(gathered[:, chunk : chunk + extra], axis=0)
    tail = jnp.concatenate([rhs_own, normal_coef.reshape(-1, BLOCK)])
    both = pair_gather(jnp.concatenate([summed[:packed_rows], tail])[None], "cov", 0)
    rhs = both[:, packed_rows : packed_rows + extra].reshape(-1)
    noise = both[:, packed_rows + extra :].reshape(-1)
    blocks = both[:, :packed_rows].reshape(2, columns, columns + half)
    order = 2 * columns
    sym = jnp.concatenate(
        [
            jnp.concatenate([blocks[0, :, :columns], jnp.zeros((columns, columns), jnp.float32)], axis=1),
            jnp.concatenate([blocks[0, :, columns:], blocks[1, :, columns:], blocks[1, :, :columns]], axis=1),
        ]
    )
    precision = 0.5 * sym + prior_precision * jnp.eye(order, dtype=jnp.float32)
    inverses, panels, forward = factor(precision, rhs)
    beta = backward(inverses, panels, forward, noise)
    beta_b = beta.astype(jnp.bfloat16)
    beta_own = lax.dynamic_slice_in_dim(beta, offset, columns)
    own_coef = lax.dynamic_slice_in_dim(beta_b, offset, columns)
    partial_eta = jnp.dot(design, own_coef, preferred_element_type=jnp.float32)
    eta = pair_sum(partial_eta, "cov")
    contrib = kappa - omega * eta
    resid_sums = segment_total(contrib, local_id, 3 * tract_dev)
    from_above = from_behind((weight_sums[:tract_dev], resid_sums[:tract_dev]), "rows", -1)
    from_below = from_behind((weight_sums[2 * tract_dev :], resid_sums[2 * tract_dev :]), "rows", 1)
    weight_total = weight_sums[tract_dev : 2 * tract_dev] + from_above[0] + from_below[0]
    resid_total = resid_sums[tract_dev : 2 * tract_dev] + from_above[1] + from_below[1]
    prec = tract_precision + weight_total
    effects = resid_total / prec + normal_tract * lax.rsqrt(prec)
    return (beta_own, effects)


def solution(mesh):
    placed = (P("rows", "cov"), P("rows"), P("rows"), P("rows"), P("rows"), P("cov"), P("rows"))
    return jax.shard_map(
        local, mesh=mesh, in_specs=placed, out_specs=(P("cov"), P("rows")), check_vma=False
    )
```

```python
import jax
import jax.numpy as jnp
from jax import lax
from jax.experimental import pallas as pl
from jax.experimental.pallas import tpu as pltpu
from jax.sharding import PartitionSpec as P

prior_precision = 1.0
tract_precision = 1.0
BLOCK = 128
HIGH = lax.Precision.HIGHEST


def extended(block, sides, width):
    for axis, dim in sides:
        count = lax.axis_size(axis)
        forward = [(i, i + 1) for i in range(count - 1)]
        backward = [(target, source) for source, target in forward]
        low = lax.ppermute(
            lax.slice_in_dim(block, block.shape[dim] - width, None, axis=dim), axis, forward
        )
        high = lax.ppermute(lax.slice_in_dim(block, 0, width, axis=dim), axis, backward)
        block = jnp.concatenate([low, block, high], axis=dim)
    return block


def from_behind(block, axis, distance):
    devices = range(lax.axis_size(axis))
    route = [(i - distance, i) for i in devices if i - distance in devices]
    return lax.ppermute(block, axis, route)


def contract_rows(left, right):
    return lax.dot_general(
        left, right, (((0,), (0,)), ((), ())), preferred_element_type=jnp.float32
    )


def mm(a, b):
    return jnp.dot(a, b, precision=HIGH, preferred_element_type=jnp.float32)


def inverse_kernel(a_ref, inv_ref, work):
    size = a_ref.shape[0]
    work[...] = a_ref[...]
    rows = lax.broadcasted_iota(jnp.int32, (size, size), 0)
    lanes = lax.broadcasted_iota(jnp.int32, (size, size), 1)
    inv_ref[...] = jnp.where(rows == lanes, 1.0, 0.0).astype(jnp.float32)
    lane = lax.broadcasted_iota(jnp.int32, (1, size), 1)
    sub = lax.broadcasted_iota(jnp.int32, (size, 1), 0)

    def step(k, carry):
        row = work[pl.ds(k, 1), :]
        pivot = jnp.sum(jnp.where(lane == k, row, 0.0), axis=1, keepdims=True)
        scale = lax.rsqrt(pivot)
        whole = work[...]
        column = jnp.sum(jnp.where(lanes == k, whole, 0.0), axis=1, keepdims=True)
        below = jnp.where(sub > k, column * scale, 0.0)
        tail = jnp.where(lane > k, row * scale, 0.0)
        work[...] = whole - below * tail
        lead = inv_ref[pl.ds(k, 1), :] * scale
        current = inv_ref[...]
        inv_ref[...] = jnp.where(rows == k, lead, current - below * lead)
        return carry

    lax.fori_loop(0, size, step, 0)


def block_inverse(block):
    size = block.shape[0]
    return pl.pallas_call(
        inverse_kernel,
        out_shape=jax.ShapeDtypeStruct((size, size), jnp.float32),
        in_specs=[pl.BlockSpec(memory_space=pltpu.VMEM)],
        out_specs=pl.BlockSpec(memory_space=pltpu.VMEM),
        scratch_shapes=[pltpu.VMEM((size, size), jnp.float32)],
        cost_estimate=pl.CostEstimate(flops=4 * size ** 3, bytes_accessed=8 * size * size, transcendentals=size),
    )(block)


def factor(precision, rhs):
    order = precision.shape[0]
    extra = jnp.zeros((8, order), jnp.float32).at[0].set(rhs)
    trailing = jnp.concatenate([precision, extra])
    inverses, panels, forward = [], [], []
    for k in range(order // BLOCK):
        inverse = block_inverse(trailing[:BLOCK, :BLOCK])
        inverses.append(inverse)
        full = mm(trailing[BLOCK:, :BLOCK], inverse.T)
        forward.append(full[-8])
        panel = full[:-8]
        if panel.shape[0]:
            panels.append(panel)
            trailing = trailing[BLOCK:, BLOCK:] - mm(full, panel.T)
    return inverses, panels, forward


def backward(inverses, panels, forward, noise):
    count = len(inverses)
    solved = []
    below = None
    for k in reversed(range(count)):
        value = forward[k] + noise[k * BLOCK : (k + 1) * BLOCK]
        if below is not None:
            value = value - mm(panels[k].T, below)
        part = mm(inverses[k].T, value)
        solved.insert(0, part)
        below = part if below is None else jnp.concatenate([part, below])
    return jnp.concatenate(solved)


def pair_gather(block, axis, dim):
    if lax.axis_size(axis) != 2:
        return lax.all_gather(block, axis, axis=dim, tiled=True)
    other = lax.ppermute(block, axis, [(0, 1), (1, 0)])
    first = lax.axis_index(axis) == 0
    return jnp.concatenate(
        [jnp.where(first, block, other), jnp.where(first, other, block)], axis=dim
    )


def pair_sum(block, axis):
    if lax.axis_size(axis) != 2:
        return lax.psum(block, axis)
    return block + lax.ppermute(block, axis, [(0, 1), (1, 0)])


def halving_sum(data, axis, late):
    count = lax.axis_size(axis)
    index = lax.axis_index(axis)
    bits = [1 << b for b in range(count.bit_length() - 1)]
    for bit in bits:
        route = [(i, i ^ bit) for i in range(count)]
        half = data.shape[0] // 2
        upper = (index & bit) != 0
        send = jnp.where(upper, data[:half], data[half:])
        keep = jnp.where(upper, data[half:], data[:half])
        data = keep + lax.ppermute(send, axis, route)
    data = jnp.concatenate([data, late])
    for bit in reversed(bits):
        route = [(i, i ^ bit) for i in range(count)]
        upper = (index & bit) != 0
        other = lax.ppermute(data, axis, route)
        data = jnp.concatenate(
            [jnp.where(upper, other, data), jnp.where(upper, data, other)]
        )
    return data.reshape(count, -1, data.shape[-1])


def one_hot(ids, size):
    return (ids[:, None] == lax.broadcasted_iota(jnp.int32, (1, size), 1)).astype(jnp.bfloat16)


def split_parts(values):
    high = lax.reduce_precision(values, exponent_bits=8, mantissa_bits=7)
    rest = values - high
    middle = lax.reduce_precision(rest, exponent_bits=8, mantissa_bits=7)
    low = rest - middle
    return jnp.stack([high, middle, low], axis=1).astype(jnp.bfloat16)


def take_rows(table, ids):
    parts = jnp.dot(one_hot(ids, table.shape[0]), split_parts(table), preferred_element_type=jnp.float32)
    return parts[:, 0] + (parts[:, 1] + parts[:, 2])


def segment_total(values, ids, size):
    parts = contract_rows(one_hot(ids, size), split_parts(values))
    return parts[:, 0] + (parts[:, 1] + parts[:, 2])


def local(design, tract_id, outcome, omega, effects_old, normal_coef, normal_tract):
    columns = design.shape[1]
    tract_dev = effects_old.shape[0]
    kappa = outcome.astype(jnp.float32) - 0.5
    window = extended(effects_old, (("rows", 0),), tract_dev)
    local_id = tract_id - (lax.axis_index("rows") - 1) * tract_dev
    effect_row = take_rows(window, local_id)
    resid = (kappa - omega * effect_row).astype(jnp.bfloat16)
    core = lax.axis_index("cov")
    offset = core * columns
    half = columns // 2
    weighted = (omega[:, None] * design).astype(jnp.bfloat16)
    whole = pair_gather(design, "cov", 1)
    whole_w = (omega[:, None] * whole).astype(jnp.bfloat16)
    own_gram = contract_rows(design, weighted)
    own_sym = own_gram + own_gram.T
    first, second = whole[:, :columns], whole[:, columns:]
    first_w, second_w = whole_w[:, :columns], whole_w[:, columns:]
    cols = lax.dynamic_slice_in_dim(first, core * half, half, axis=1)
    cols_w = lax.dynamic_slice_in_dim(first_w, core * half, half, axis=1)
    cross = contract_rows(second, cols_w) + contract_rows(cols, second_w).T
    rhs_block = contract_rows(resid, design)
    weight_sums = segment_total(omega, local_id, 3 * tract_dev)
    packed = jnp.concatenate([own_sym, cross], axis=1).reshape(-1, BLOCK)
    packed_rows = packed.shape[0]
    extra = columns // BLOCK
    count = lax.axis_size("rows")
    unit = 8 * count
    total = -(-packed_rows // unit) * unit
    if total > packed_rows:
        packed = jnp.concatenate([packed, jnp.zeros((total - packed_rows, BLOCK), jnp.float32)])
    late_rows = -(-extra // 8) * 8
    late = jnp.concatenate(
        [rhs_block.reshape(-1, BLOCK), jnp.zeros((late_rows - extra, BLOCK), jnp.float32)]
    ) + 0.0 * weight_sums[0]
    gathered = halving_sum(packed, "rows", late)
    chunk = total // count
    summed = gathered[:, :chunk].reshape(total, BLOCK)
    rhs_own = jnp.sum(gathered[:, chunk : chunk + extra], axis=0)
    tail = jnp.concatenate([rhs_own, normal_coef.reshape(-1, BLOCK)])
    both = pair_gather(jnp.concatenate([summed[:packed_rows], tail])[None], "cov", 0)
    rhs = both[:, packed_rows : packed_rows + extra].reshape(-1)
    noise = both[:, packed_rows + extra :].reshape(-1)
    blocks = both[:, :packed_rows].reshape(2, columns, columns + half)
    order = 2 * columns
    sym = jnp.concatenate(
        [
            jnp.concatenate([blocks[0, :, :columns], jnp.zeros((columns, columns), jnp.float32)], axis=1),
            jnp.concatenate([blocks[0, :, columns:], blocks[1, :, columns:], blocks[1, :, :columns]], axis=1),
        ]
    )
    precision = 0.5 * sym + prior_precision * jnp.eye(order, dtype=jnp.float32)
    inverses, panels, forward = factor(precision, rhs)
    beta = backward(inverses, panels, forward, noise)
    beta_b = beta.astype(jnp.bfloat16)
    beta_own = lax.dynamic_slice_in_dim(beta, offset, columns)
    own_coef = lax.dynamic_slice_in_dim(beta_b, offset, columns)
    partial_eta = jnp.dot(design, own_coef, preferred_element_type=jnp.float32)
    eta = pair_sum(partial_eta, "cov")
    contrib = kappa - omega * eta
    resid_sums = segment_total(contrib, local_id, 3 * tract_dev)
    from_above = from_behind((weight_sums[:tract_dev], resid_sums[:tract_dev]), "rows", -1)
    from_below = from_behind((weight_sums[2 * tract_dev :], resid_sums[2 * tract_dev :]), "rows", 1)
    weight_total = weight_sums[tract_dev : 2 * tract_dev] + from_above[0] + from_below[0]
    resid_total = resid_sums[tract_dev : 2 * tract_dev] + from_above[1] + from_below[1]
    prec = tract_precision + weight_total
    effects = resid_total / prec + normal_tract * lax.rsqrt(prec)
    return (beta_own, effects)


def solution(mesh):
    placed = (P("rows", "cov"), P("rows"), P("rows"), P("rows"), P("rows"), P("cov"), P("rows"))
    return jax.shard_map(
        local, mesh=mesh, in_specs=placed, out_specs=(P("cov"), P("rows")), check_vma=False
    )
```

```python
import jax
import jax.numpy as jnp
from jax import lax
from jax.experimental import pallas as pl
from jax.experimental.pallas import tpu as pltpu
from jax.sharding import PartitionSpec as P

prior_precision = 1.0
tract_precision = 1.0
BLOCK = 128
HIGH = lax.Precision.HIGHEST


def extended(block, sides, width):
    for axis, dim in sides:
        count = lax.axis_size(axis)
        forward = [(i, i + 1) for i in range(count - 1)]
        backward = [(target, source) for source, target in forward]
        low = lax.ppermute(
            lax.slice_in_dim(block, block.shape[dim] - width, None, axis=dim), axis, forward
        )
        high = lax.ppermute(lax.slice_in_dim(block, 0, width, axis=dim), axis, backward)
        block = jnp.concatenate([low, block, high], axis=dim)
    return block


def from_behind(block, axis, distance):
    devices = range(lax.axis_size(axis))
    route = [(i - distance, i) for i in devices if i - distance in devices]
    return lax.ppermute(block, axis, route)


def contract_rows(left, right):
    return lax.dot_general(
        left, right, (((0,), (0,)), ((), ())), preferred_element_type=jnp.float32
    )


def mm(a, b):
    return jnp.dot(a, b, precision=HIGH, preferred_element_type=jnp.float32)


def inverse_kernel(a_ref, inv_ref, work):
    size = a_ref.shape[0]
    work[...] = a_ref[...]
    rows = lax.broadcasted_iota(jnp.int32, (size, size), 0)
    lanes = lax.broadcasted_iota(jnp.int32, (size, size), 1)
    inv_ref[...] = jnp.where(rows == lanes, 1.0, 0.0).astype(jnp.float32)
    lane = lax.broadcasted_iota(jnp.int32, (1, size), 1)
    sub = lax.broadcasted_iota(jnp.int32, (size, 1), 0)

    def step(k, carry):
        row = work[pl.ds(k, 1), :]
        pivot = jnp.sum(jnp.where(lane == k, row, 0.0), axis=1, keepdims=True)
        scale = lax.rsqrt(pivot)
        whole = work[...]
        column = jnp.sum(jnp.where(lanes == k, whole, 0.0), axis=1, keepdims=True)
        below = jnp.where(sub > k, column * scale, 0.0)
        tail = jnp.where(lane > k, row * scale, 0.0)
        work[...] = whole - below * tail
        lead = inv_ref[pl.ds(k, 1), :] * scale
        current = inv_ref[...]
        inv_ref[...] = jnp.where(rows == k, lead, current - below * lead)
        return carry

    lax.fori_loop(0, size, step, 0)


def block_inverse(block):
    size = block.shape[0]
    return pl.pallas_call(
        inverse_kernel,
        out_shape=jax.ShapeDtypeStruct((size, size), jnp.float32),
        in_specs=[pl.BlockSpec(memory_space=pltpu.VMEM)],
        out_specs=pl.BlockSpec(memory_space=pltpu.VMEM),
        scratch_shapes=[pltpu.VMEM((size, size), jnp.float32)],
        cost_estimate=pl.CostEstimate(flops=4 * size ** 3, bytes_accessed=8 * size * size, transcendentals=size),
    )(block)


def factor(precision, rhs):
    order = precision.shape[0]
    extra = jnp.zeros((8, order), jnp.float32).at[0].set(rhs)
    trailing = jnp.concatenate([precision, extra])
    inverses, panels, forward = [], [], []
    for k in range(order // BLOCK):
        inverse = block_inverse(trailing[:BLOCK, :BLOCK])
        inverses.append(inverse)
        full = mm(trailing[BLOCK:, :BLOCK], inverse.T)
        forward.append(full[-8])
        panel = full[:-8]
        if panel.shape[0]:
            panels.append(panel)
            trailing = trailing[BLOCK:, BLOCK:] - mm(full, panel.T)
    return inverses, panels, forward


def backward(inverses, panels, forward, noise):
    count = len(inverses)
    solved = []
    below = None
    for k in reversed(range(count)):
        value = forward[k] + noise[k * BLOCK : (k + 1) * BLOCK]
        if below is not None:
            value = value - mm(panels[k].T, below)
        part = mm(inverses[k].T, value)
        solved.insert(0, part)
        below = part if below is None else jnp.concatenate([part, below])
    return jnp.concatenate(solved)


def pair_gather(block, axis, dim):
    if lax.axis_size(axis) != 2:
        return lax.all_gather(block, axis, axis=dim, tiled=True)
    other = lax.ppermute(block, axis, [(0, 1), (1, 0)])
    first = lax.axis_index(axis) == 0
    return jnp.concatenate(
        [jnp.where(first, block, other), jnp.where(first, other, block)], axis=dim
    )


def pair_sum(block, axis):
    if lax.axis_size(axis) != 2:
        return lax.psum(block, axis)
    return block + lax.ppermute(block, axis, [(0, 1), (1, 0)])


def group_steps(count):
    bits = [1 << b for b in range(count.bit_length() - 1)]
    return [bits[i : i + 2] for i in range(0, len(bits), 2)]


def group_position(index, group):
    return sum(((index & bit) != 0).astype(jnp.int32) << j for j, bit in enumerate(group))


def partner_mask(group, m):
    return sum(bit for j, bit in enumerate(group) if (m >> j) & 1)


def halving_sum(data, axis, late):
    count = lax.axis_size(axis)
    index = lax.axis_index(axis)
    groups = group_steps(count)
    for group in groups:
        size = 1 << len(group)
        piece = data.shape[0] // size
        place = group_position(index, group)
        total = lax.dynamic_slice_in_dim(data, place * piece, piece)
        for m in range(1, size):
            mask = partner_mask(group, m)
            route = [(i, i ^ mask) for i in range(count)]
            send = lax.dynamic_slice_in_dim(data, (place ^ m) * piece, piece)
            total = total + lax.ppermute(send, axis, route)
        data = total
    data = jnp.concatenate([data, late])
    for group in reversed(groups):
        size = 1 << len(group)
        place = group_position(index, group)
        got = [data]
        for m in range(1, size):
            mask = partner_mask(group, m)
            route = [(i, i ^ mask) for i in range(count)]
            got.append(lax.ppermute(data, axis, route))
        slots = []
        for j in range(size):
            value = got[0]
            for m in range(1, size):
                value = jnp.where((place ^ m) == j, got[m], value)
            slots.append(value)
        data = jnp.concatenate(slots)
    return data.reshape(count, -1, data.shape[-1])


def one_hot(ids, size):
    return (ids[:, None] == lax.broadcasted_iota(jnp.int32, (1, size), 1)).astype(jnp.bfloat16)


def split_parts(values):
    high = lax.reduce_precision(values, exponent_bits=8, mantissa_bits=7)
    rest = values - high
    middle = lax.reduce_precision(rest, exponent_bits=8, mantissa_bits=7)
    low = rest - middle
    return jnp.stack([high, middle, low], axis=1).astype(jnp.bfloat16)


def take_rows(table, ids):
    parts = jnp.dot(one_hot(ids, table.shape[0]), split_parts(table), preferred_element_type=jnp.float32)
    return parts[:, 0] + (parts[:, 1] + parts[:, 2])


def segment_total(values, ids, size):
    parts = contract_rows(one_hot(ids, size), split_parts(values))
    return parts[:, 0] + (parts[:, 1] + parts[:, 2])


def local(design, tract_id, outcome, omega, effects_old, normal_coef, normal_tract):
    columns = design.shape[1]
    tract_dev = effects_old.shape[0]
    kappa = outcome.astype(jnp.float32) - 0.5
    window = extended(effects_old, (("rows", 0),), tract_dev)
    local_id = tract_id - (lax.axis_index("rows") - 1) * tract_dev
    effect_row = take_rows(window, local_id)
    resid = (kappa - omega * effect_row).astype(jnp.bfloat16)
    core = lax.axis_index("cov")
    offset = core * columns
    half = columns // 2
    weighted = (omega[:, None] * design).astype(jnp.bfloat16)
    whole = pair_gather(design, "cov", 1)
    whole_w = (omega[:, None] * whole).astype(jnp.bfloat16)
    own_gram = contract_rows(design, weighted)
    own_sym = own_gram + own_gram.T
    first, second = whole[:, :columns], whole[:, columns:]
    first_w, second_w = whole_w[:, :columns], whole_w[:, columns:]
    cols = lax.dynamic_slice_in_dim(first, core * half, half, axis=1)
    cols_w = lax.dynamic_slice_in_dim(first_w, core * half, half, axis=1)
    cross = contract_rows(second, cols_w) + contract_rows(cols, second_w).T
    rhs_block = contract_rows(resid, design)
    weight_sums = segment_total(omega, local_id, 3 * tract_dev)
    packed = jnp.concatenate([own_sym, cross], axis=1).reshape(-1, BLOCK)
    packed_rows = packed.shape[0]
    extra = columns // BLOCK
    count = lax.axis_size("rows")
    unit = 8 * count
    total = -(-packed_rows // unit) * unit
    if total > packed_rows:
        packed = jnp.concatenate([packed, jnp.zeros((total - packed_rows, BLOCK), jnp.float32)])
    late_rows = -(-extra // 8) * 8
    late = jnp.concatenate(
        [rhs_block.reshape(-1, BLOCK), jnp.zeros((late_rows - extra, BLOCK), jnp.float32)]
    ) + 0.0 * weight_sums[0]
    gathered = halving_sum(packed, "rows", late)
    chunk = total // count
    summed = gathered[:, :chunk].reshape(total, BLOCK)
    rhs_own = jnp.sum(gathered[:, chunk : chunk + extra], axis=0)
    tail = jnp.concatenate([rhs_own, normal_coef.reshape(-1, BLOCK)])
    both = pair_gather(jnp.concatenate([summed[:packed_rows], tail])[None], "cov", 0)
    rhs = both[:, packed_rows : packed_rows + extra].reshape(-1)
    noise = both[:, packed_rows + extra :].reshape(-1)
    blocks = both[:, :packed_rows].reshape(2, columns, columns + half)
    order = 2 * columns
    sym = jnp.concatenate(
        [
            jnp.concatenate([blocks[0, :, :columns], jnp.zeros((columns, columns), jnp.float32)], axis=1),
            jnp.concatenate([blocks[0, :, columns:], blocks[1, :, columns:], blocks[1, :, :columns]], axis=1),
        ]
    )
    precision = 0.5 * sym + prior_precision * jnp.eye(order, dtype=jnp.float32)
    inverses, panels, forward = factor(precision, rhs)
    beta = backward(inverses, panels, forward, noise)
    beta_b = beta.astype(jnp.bfloat16)
    beta_own = lax.dynamic_slice_in_dim(beta, offset, columns)
    own_coef = lax.dynamic_slice_in_dim(beta_b, offset, columns)
    partial_eta = jnp.dot(design, own_coef, preferred_element_type=jnp.float32)
    eta = pair_sum(partial_eta, "cov")
    contrib = kappa - omega * eta
    resid_sums = segment_total(contrib, local_id, 3 * tract_dev)
    from_above = from_behind((weight_sums[:tract_dev], resid_sums[:tract_dev]), "rows", -1)
    from_below = from_behind((weight_sums[2 * tract_dev :], resid_sums[2 * tract_dev :]), "rows", 1)
    weight_total = weight_sums[tract_dev : 2 * tract_dev] + from_above[0] + from_below[0]
    resid_total = resid_sums[tract_dev : 2 * tract_dev] + from_above[1] + from_below[1]
    prec = tract_precision + weight_total
    effects = resid_total / prec + normal_tract * lax.rsqrt(prec)
    return (beta_own, effects)


def solution(mesh):
    placed = (P("rows", "cov"), P("rows"), P("rows"), P("rows"), P("rows"), P("cov"), P("rows"))
    return jax.shard_map(
        local, mesh=mesh, in_specs=placed, out_specs=(P("cov"), P("rows")), check_vma=False
    )
```

```python
import jax
import jax.numpy as jnp
from jax import lax
from jax.experimental import pallas as pl
from jax.experimental.pallas import tpu as pltpu
from jax.sharding import PartitionSpec as P

prior_precision = 1.0
tract_precision = 1.0
BLOCK = 128
HIGH = lax.Precision.HIGHEST


def extended(block, sides, width):
    for axis, dim in sides:
        count = lax.axis_size(axis)
        forward = [(i, i + 1) for i in range(count - 1)]
        backward = [(target, source) for source, target in forward]
        low = lax.ppermute(
            lax.slice_in_dim(block, block.shape[dim] - width, None, axis=dim), axis, forward
        )
        high = lax.ppermute(lax.slice_in_dim(block, 0, width, axis=dim), axis, backward)
        block = jnp.concatenate([low, block, high], axis=dim)
    return block


def from_behind(block, axis, distance):
    devices = range(lax.axis_size(axis))
    route = [(i - distance, i) for i in devices if i - distance in devices]
    return lax.ppermute(block, axis, route)


def contract_rows(left, right):
    return lax.dot_general(
        left, right, (((0,), (0,)), ((), ())), preferred_element_type=jnp.float32
    )


def mm(a, b):
    return jnp.dot(a, b, precision=HIGH, preferred_element_type=jnp.float32)


def inverse_kernel(a_ref, inv_ref, work):
    size = a_ref.shape[0]
    work[...] = a_ref[...]
    rows = lax.broadcasted_iota(jnp.int32, (size, size), 0)
    lanes = lax.broadcasted_iota(jnp.int32, (size, size), 1)
    inv_ref[...] = jnp.where(rows == lanes, 1.0, 0.0).astype(jnp.float32)
    lane = lax.broadcasted_iota(jnp.int32, (1, size), 1)
    sub = lax.broadcasted_iota(jnp.int32, (size, 1), 0)

    def step(k, carry):
        row = work[pl.ds(k, 1), :]
        pivot = jnp.sum(jnp.where(lane == k, row, 0.0), axis=1, keepdims=True)
        scale = lax.rsqrt(pivot)
        whole = work[...]
        column = jnp.sum(jnp.where(lanes == k, whole, 0.0), axis=1, keepdims=True)
        below = jnp.where(sub > k, column * scale, 0.0)
        tail = jnp.where(lane > k, row * scale, 0.0)
        work[...] = whole - below * tail
        lead = inv_ref[pl.ds(k, 1), :] * scale
        current = inv_ref[...]
        inv_ref[...] = jnp.where(rows == k, lead, current - below * lead)
        return carry

    lax.fori_loop(0, size, step, 0)


def block_inverse(block):
    size = block.shape[0]
    return pl.pallas_call(
        inverse_kernel,
        out_shape=jax.ShapeDtypeStruct((size, size), jnp.float32),
        in_specs=[pl.BlockSpec(memory_space=pltpu.VMEM)],
        out_specs=pl.BlockSpec(memory_space=pltpu.VMEM),
        scratch_shapes=[pltpu.VMEM((size, size), jnp.float32)],
        cost_estimate=pl.CostEstimate(flops=4 * size ** 3, bytes_accessed=8 * size * size, transcendentals=size),
    )(block)


def factor(precision, rhs):
    order = precision.shape[0]
    extra = jnp.zeros((8, order), jnp.float32).at[0].set(rhs)
    trailing = jnp.concatenate([precision, extra])
    inverses, panels, forward = [], [], []
    for k in range(order // BLOCK):
        inverse = block_inverse(trailing[:BLOCK, :BLOCK])
        inverses.append(inverse)
        full = mm(trailing[BLOCK:, :BLOCK], inverse.T)
        forward.append(full[-8])
        panel = full[:-8]
        if panel.shape[0]:
            panels.append(panel)
            trailing = trailing[BLOCK:, BLOCK:] - mm(full, panel.T)
    return inverses, panels, forward


def backward(inverses, panels, forward, noise):
    count = len(inverses)
    solved = jnp.zeros((count * BLOCK,), jnp.float32)
    for k in reversed(range(count)):
        value = forward[k] + noise[k * BLOCK : (k + 1) * BLOCK]
        if k < count - 1:
            value = value - mm(panels[k].T, solved[(k + 1) * BLOCK :])
        solved = solved.at[k * BLOCK : (k + 1) * BLOCK].set(mm(inverses[k].T, value))
    return solved


def pair_gather(block, axis, dim):
    if lax.axis_size(axis) != 2:
        return lax.all_gather(block, axis, axis=dim, tiled=True)
    other = lax.ppermute(block, axis, [(0, 1), (1, 0)])
    first = lax.axis_index(axis) == 0
    return jnp.concatenate(
        [jnp.where(first, block, other), jnp.where(first, other, block)], axis=dim
    )


def pair_sum(block, axis):
    if lax.axis_size(axis) != 2:
        return lax.psum(block, axis)
    return block + lax.ppermute(block, axis, [(0, 1), (1, 0)])


def halving_sum(data, axis, late):
    count = lax.axis_size(axis)
    index = lax.axis_index(axis)
    bits = [1 << b for b in range(count.bit_length() - 1)]
    for bit in bits:
        route = [(i, i ^ bit) for i in range(count)]
        half = data.shape[0] // 2
        upper = (index & bit) != 0
        send = jnp.where(upper, data[:half], data[half:])
        keep = jnp.where(upper, data[half:], data[:half])
        data = keep + lax.ppermute(send, axis, route)
    data = jnp.concatenate([data, late])
    for bit in reversed(bits):
        route = [(i, i ^ bit) for i in range(count)]
        upper = (index & bit) != 0
        other = lax.ppermute(data, axis, route)
        data = jnp.concatenate(
            [jnp.where(upper, other, data), jnp.where(upper, data, other)]
        )
    return data.reshape(count, -1, data.shape[-1])


def one_hot(ids, size):
    return (ids[:, None] == lax.broadcasted_iota(jnp.int32, (1, size), 1)).astype(jnp.bfloat16)


def split_parts(values):
    high = lax.reduce_precision(values, exponent_bits=8, mantissa_bits=7)
    rest = values - high
    middle = lax.reduce_precision(rest, exponent_bits=8, mantissa_bits=7)
    low = rest - middle
    return jnp.stack([high, middle, low], axis=1).astype(jnp.bfloat16)


def take_rows(table, ids):
    parts = jnp.dot(one_hot(ids, table.shape[0]), split_parts(table), preferred_element_type=jnp.float32)
    return parts[:, 0] + (parts[:, 1] + parts[:, 2])


def segment_total(values, ids, size):
    parts = contract_rows(one_hot(ids, size), split_parts(values))
    return parts[:, 0] + (parts[:, 1] + parts[:, 2])


def local(design, tract_id, outcome, omega, effects_old, normal_coef, normal_tract):
    columns = design.shape[1]
    tract_dev = effects_old.shape[0]
    kappa = outcome.astype(jnp.float32) - 0.5
    window = extended(effects_old, (("rows", 0),), tract_dev)
    local_id = tract_id - (lax.axis_index("rows") - 1) * tract_dev
    effect_row = take_rows(window, local_id)
    resid = (kappa - omega * effect_row).astype(jnp.bfloat16)
    core = lax.axis_index("cov")
    offset = core * columns
    half = columns // 2
    weighted = (omega[:, None] * design).astype(jnp.bfloat16)
    whole = pair_gather(design, "cov", 1)
    whole_w = (omega[:, None] * whole).astype(jnp.bfloat16)
    own_gram = contract_rows(design, weighted)
    own_sym = own_gram + own_gram.T
    first, second = whole[:, :columns], whole[:, columns:]
    first_w, second_w = whole_w[:, :columns], whole_w[:, columns:]
    cols = lax.dynamic_slice_in_dim(first, core * half, half, axis=1)
    cols_w = lax.dynamic_slice_in_dim(first_w, core * half, half, axis=1)
    cross = contract_rows(second, cols_w) + contract_rows(cols, second_w).T
    rhs_block = contract_rows(resid, design)
    weight_sums = segment_total(omega, local_id, 3 * tract_dev)
    packed = jnp.concatenate([own_sym, cross], axis=1).reshape(-1, BLOCK)
    packed_rows = packed.shape[0]
    extra = columns // BLOCK
    count = lax.axis_size("rows")
    unit = 8 * count
    total = -(-packed_rows // unit) * unit
    if total > packed_rows:
        packed = jnp.concatenate([packed, jnp.zeros((total - packed_rows, BLOCK), jnp.float32)])
    late_rows = -(-extra // 8) * 8
    late = jnp.concatenate(
        [rhs_block.reshape(-1, BLOCK), jnp.zeros((late_rows - extra, BLOCK), jnp.float32)]
    ) + 0.0 * weight_sums[0]
    gathered = halving_sum(packed, "rows", late)
    chunk = total // count
    summed = gathered[:, :chunk].reshape(total, BLOCK)
    rhs_own = jnp.sum(gathered[:, chunk : chunk + extra], axis=0)
    tail = jnp.concatenate([rhs_own, normal_coef.reshape(-1, BLOCK)])
    both = pair_gather(jnp.concatenate([summed[:packed_rows], tail])[None], "cov", 0)
    rhs = both[:, packed_rows : packed_rows + extra].reshape(-1)
    noise = both[:, packed_rows + extra :].reshape(-1)
    blocks = both[:, :packed_rows].reshape(2, columns, columns + half)
    order = 2 * columns
    sym = jnp.concatenate(
        [
            jnp.concatenate([blocks[0, :, :columns], jnp.zeros((columns, columns), jnp.float32)], axis=1),
            jnp.concatenate([blocks[0, :, columns:], blocks[1, :, columns:], blocks[1, :, :columns]], axis=1),
        ]
    )
    precision = 0.5 * sym + prior_precision * jnp.eye(order, dtype=jnp.float32)
    inverses, panels, forward = factor(precision, rhs)
    beta = backward(inverses, panels, forward, noise)
    beta_b = beta.astype(jnp.bfloat16)
    beta_own = lax.dynamic_slice_in_dim(beta, offset, columns)
    own_coef = lax.dynamic_slice_in_dim(beta_b, offset, columns)
    partial_eta = jnp.dot(design, own_coef, preferred_element_type=jnp.float32)
    eta = pair_sum(partial_eta, "cov")
    contrib = kappa - omega * eta
    resid_sums = segment_total(contrib, local_id, 3 * tract_dev)
    from_above = from_behind((weight_sums[:tract_dev], resid_sums[:tract_dev]), "rows", -1)
    from_below = from_behind((weight_sums[2 * tract_dev :], resid_sums[2 * tract_dev :]), "rows", 1)
    weight_total = weight_sums[tract_dev : 2 * tract_dev] + from_above[0] + from_below[0]
    resid_total = resid_sums[tract_dev : 2 * tract_dev] + from_above[1] + from_below[1]
    prec = tract_precision + weight_total
    effects = resid_total / prec + normal_tract * lax.rsqrt(prec)
    return (beta_own, effects)


def solution(mesh):
    placed = (P("rows", "cov"), P("rows"), P("rows"), P("rows"), P("rows"), P("cov"), P("rows"))
    return jax.shard_map(
        local, mesh=mesh, in_specs=placed, out_specs=(P("cov"), P("rows")), check_vma=False
    )
```

```python
import jax
import jax.numpy as jnp
from jax import lax
from jax.experimental import pallas as pl
from jax.experimental.pallas import tpu as pltpu
from jax.sharding import PartitionSpec as P

prior_precision = 1.0
tract_precision = 1.0
BLOCK = 128
HIGH = lax.Precision.HIGHEST


def extended(block, sides, width):
    for axis, dim in sides:
        count = lax.axis_size(axis)
        forward = [(i, i + 1) for i in range(count - 1)]
        backward = [(target, source) for source, target in forward]
        low = lax.ppermute(
            lax.slice_in_dim(block, block.shape[dim] - width, None, axis=dim), axis, forward
        )
        high = lax.ppermute(lax.slice_in_dim(block, 0, width, axis=dim), axis, backward)
        block = jnp.concatenate([low, block, high], axis=dim)
    return block


def from_behind(block, axis, distance):
    devices = range(lax.axis_size(axis))
    route = [(i - distance, i) for i in devices if i - distance in devices]
    return lax.ppermute(block, axis, route)


def contract_rows(left, right):
    return lax.dot_general(
        left, right, (((0,), (0,)), ((), ())), preferred_element_type=jnp.float32
    )


def mm(a, b):
    return jnp.dot(a, b, precision=HIGH, preferred_element_type=jnp.float32)


def inverse_kernel(a_ref, inv_ref, work):
    size = a_ref.shape[0]
    work[...] = a_ref[...]
    rows = lax.broadcasted_iota(jnp.int32, (size, size), 0)
    lanes = lax.broadcasted_iota(jnp.int32, (size, size), 1)
    inv_ref[...] = jnp.where(rows == lanes, 1.0, 0.0).astype(jnp.float32)
    lane = lax.broadcasted_iota(jnp.int32, (1, size), 1)
    sub = lax.broadcasted_iota(jnp.int32, (size, 1), 0)

    def step(k, carry):
        row = work[pl.ds(k, 1), :]
        pivot = jnp.sum(jnp.where(lane == k, row, 0.0), axis=1, keepdims=True)
        scale = lax.rsqrt(pivot)
        whole = work[...]
        column = jnp.sum(jnp.where(lanes == k, whole, 0.0), axis=1, keepdims=True)
        below = jnp.where(sub > k, column * scale, 0.0)
        tail = jnp.where(lane > k, row * scale, 0.0)
        work[...] = whole - below * tail
        lead = inv_ref[pl.ds(k, 1), :] * scale
        current = inv_ref[...]
        inv_ref[...] = jnp.where(rows == k, lead, current - below * lead)
        return carry

    lax.fori_loop(0, size, step, 0)


def block_inverse(block):
    size = block.shape[0]
    return pl.pallas_call(
        inverse_kernel,
        out_shape=jax.ShapeDtypeStruct((size, size), jnp.float32),
        in_specs=[pl.BlockSpec(memory_space=pltpu.VMEM)],
        out_specs=pl.BlockSpec(memory_space=pltpu.VMEM),
        scratch_shapes=[pltpu.VMEM((size, size), jnp.float32)],
        cost_estimate=pl.CostEstimate(flops=4 * size ** 3, bytes_accessed=8 * size * size, transcendentals=size),
    )(block)


def factor(precision, rhs):
    order = precision.shape[0]
    extra = jnp.zeros((8, order), jnp.float32).at[0].set(rhs)
    trailing = jnp.concatenate([precision, extra])
    inverses, panels, forward = [], [], []
    for k in range(order // BLOCK):
        inverse = block_inverse(trailing[:BLOCK, :BLOCK])
        inverses.append(inverse)
        full = mm(trailing[BLOCK:, :BLOCK], inverse.T)
        forward.append(full[-8])
        panel = full[:-8]
        if panel.shape[0]:
            panels.append(panel)
            trailing = trailing[BLOCK:, BLOCK:] - mm(full, panel.T)
    return inverses, panels, forward


def backward(inverses, panels, forward, noise):
    count = len(inverses)
    solved = jnp.zeros((count * BLOCK,), jnp.float32)
    for k in reversed(range(count)):
        value = forward[k] + noise[k * BLOCK : (k + 1) * BLOCK]
        if k < count - 1:
            value = value - mm(panels[k].T, solved[(k + 1) * BLOCK :])
        solved = solved.at[k * BLOCK : (k + 1) * BLOCK].set(mm(inverses[k].T, value))
    return solved


def pair_gather(block, axis, dim):
    if lax.axis_size(axis) != 2:
        return lax.all_gather(block, axis, axis=dim, tiled=True)
    other = lax.ppermute(block, axis, [(0, 1), (1, 0)])
    first = lax.axis_index(axis) == 0
    return jnp.concatenate(
        [jnp.where(first, block, other), jnp.where(first, other, block)], axis=dim
    )


def pair_sum(block, axis):
    if lax.axis_size(axis) != 2:
        return lax.psum(block, axis)
    return block + lax.ppermute(block, axis, [(0, 1), (1, 0)])


def halving_sum(data, axis, late):
    count = lax.axis_size(axis)
    index = lax.axis_index(axis)
    bits = [1 << b for b in range(count.bit_length() - 1)]
    for bit in bits:
        route = [(i, i ^ bit) for i in range(count)]
        half = data.shape[0] // 2
        upper = (index & bit) != 0
        send = jnp.where(upper, data[:half], data[half:])
        keep = jnp.where(upper, data[half:], data[:half])
        data = keep + lax.ppermute(send, axis, route)
    data = jnp.concatenate([data, late])
    for bit in reversed(bits):
        route = [(i, i ^ bit) for i in range(count)]
        upper = (index & bit) != 0
        other = lax.ppermute(data, axis, route)
        data = jnp.concatenate(
            [jnp.where(upper, other, data), jnp.where(upper, data, other)]
        )
    return data.reshape(count, -1, data.shape[-1])


def one_hot(ids, size):
    return (ids[:, None] == lax.broadcasted_iota(jnp.int32, (1, size), 1)).astype(jnp.bfloat16)


def split_parts(values):
    high = lax.reduce_precision(values, exponent_bits=8, mantissa_bits=7)
    rest = values - high
    middle = lax.reduce_precision(rest, exponent_bits=8, mantissa_bits=7)
    low = rest - middle
    return jnp.stack([high, middle, low], axis=1).astype(jnp.bfloat16)


def take_rows(table, ids):
    parts = jnp.dot(one_hot(ids, table.shape[0]), split_parts(table), preferred_element_type=jnp.float32)
    return parts[:, 0] + (parts[:, 1] + parts[:, 2])


def segment_total(values, ids, size):
    parts = contract_rows(one_hot(ids, size), split_parts(values))
    return parts[:, 0] + (parts[:, 1] + parts[:, 2])


def local(design, tract_id, outcome, omega, effects_old, normal_coef, normal_tract):
    columns = design.shape[1]
    tract_dev = effects_old.shape[0]
    kappa = outcome.astype(jnp.float32) - 0.5
    window = extended(effects_old, (("rows", 0),), tract_dev)
    local_id = tract_id - (lax.axis_index("rows") - 1) * tract_dev
    effect_row = take_rows(window, local_id)
    resid = (kappa - omega * effect_row).astype(jnp.bfloat16)
    core = lax.axis_index("cov")
    offset = core * columns
    half = columns // 2
    weighted = (omega[:, None] * design).astype(jnp.bfloat16)
    whole = pair_gather(design, "cov", 1)
    whole_w = (omega[:, None] * whole).astype(jnp.bfloat16)
    own_gram = contract_rows(design, weighted)
    own_sym = own_gram + own_gram.T
    first, second = whole[:, :columns], whole[:, columns:]
    first_w, second_w = whole_w[:, :columns], whole_w[:, columns:]
    cols = lax.dynamic_slice_in_dim(first, core * half, half, axis=1)
    cols_w = lax.dynamic_slice_in_dim(first_w, core * half, half, axis=1)
    cross = contract_rows(second, cols_w) + contract_rows(cols, second_w).T
    rhs_block = contract_rows(resid, design)
    weight_sums = segment_total(omega, local_id, 3 * tract_dev)
    sides = jnp.concatenate([own_sym, cross], axis=1)
    packed = jnp.concatenate(
        [sides[:, j * BLOCK : (j + 1) * BLOCK] for j in range(sides.shape[1] // BLOCK)]
    )
    packed_rows = packed.shape[0]
    extra = columns // BLOCK
    count = lax.axis_size("rows")
    unit = 8 * count
    total = -(-packed_rows // unit) * unit
    if total > packed_rows:
        packed = jnp.concatenate([packed, jnp.zeros((total - packed_rows, BLOCK), jnp.float32)])
    late_rows = -(-extra // 8) * 8
    late = jnp.concatenate(
        [rhs_block.reshape(-1, BLOCK), jnp.zeros((late_rows - extra, BLOCK), jnp.float32)]
    ) + 0.0 * weight_sums[0]
    gathered = halving_sum(packed, "rows", late)
    chunk = total // count
    summed = gathered[:, :chunk].reshape(total, BLOCK)
    rhs_own = jnp.sum(gathered[:, chunk : chunk + extra], axis=0)
    tail = jnp.concatenate([rhs_own, normal_coef.reshape(-1, BLOCK)])
    both = pair_gather(jnp.concatenate([summed[:packed_rows], tail])[None], "cov", 0)
    rhs = both[:, packed_rows : packed_rows + extra].reshape(-1)
    noise = both[:, packed_rows + extra :].reshape(-1)
    strips = both[:, :packed_rows].reshape(2, -1, columns, BLOCK)
    per = columns // BLOCK
    order = 2 * columns
    sym = jnp.concatenate(
        [
            jnp.concatenate([strips[0, t] for t in range(per)] + [jnp.zeros((columns, columns), jnp.float32)], axis=1),
            jnp.concatenate(
                [strips[0, per + t] for t in range(half // BLOCK)]
                + [strips[1, per + t] for t in range(half // BLOCK)]
                + [strips[1, t] for t in range(per)],
                axis=1,
            ),
        ]
    )
    precision = 0.5 * sym + prior_precision * jnp.eye(order, dtype=jnp.float32)
    inverses, panels, forward = factor(precision, rhs)
    beta = backward(inverses, panels, forward, noise)
    beta_b = beta.astype(jnp.bfloat16)
    beta_own = lax.dynamic_slice_in_dim(beta, offset, columns)
    own_coef = lax.dynamic_slice_in_dim(beta_b, offset, columns)
    partial_eta = jnp.dot(design, own_coef, preferred_element_type=jnp.float32)
    eta = pair_sum(partial_eta, "cov")
    contrib = kappa - omega * eta
    resid_sums = segment_total(contrib, local_id, 3 * tract_dev)
    from_above = from_behind((weight_sums[:tract_dev], resid_sums[:tract_dev]), "rows", -1)
    from_below = from_behind((weight_sums[2 * tract_dev :], resid_sums[2 * tract_dev :]), "rows", 1)
    weight_total = weight_sums[tract_dev : 2 * tract_dev] + from_above[0] + from_below[0]
    resid_total = resid_sums[tract_dev : 2 * tract_dev] + from_above[1] + from_below[1]
    prec = tract_precision + weight_total
    effects = resid_total / prec + normal_tract * lax.rsqrt(prec)
    return (beta_own, effects)


def solution(mesh):
    placed = (P("rows", "cov"), P("rows"), P("rows"), P("rows"), P("rows"), P("cov"), P("rows"))
    return jax.shard_map(
        local, mesh=mesh, in_specs=placed, out_specs=(P("cov"), P("rows")), check_vma=False
    )
```

```python
import jax
import jax.numpy as jnp
from jax import lax
from jax.experimental import pallas as pl
from jax.experimental.pallas import tpu as pltpu
from jax.sharding import PartitionSpec as P

prior_precision = 1.0
tract_precision = 1.0
BLOCK = 128
HIGH = lax.Precision.HIGHEST


def extended(block, sides, width):
    for axis, dim in sides:
        count = lax.axis_size(axis)
        forward = [(i, i + 1) for i in range(count - 1)]
        backward = [(target, source) for source, target in forward]
        low = lax.ppermute(
            lax.slice_in_dim(block, block.shape[dim] - width, None, axis=dim), axis, forward
        )
        high = lax.ppermute(lax.slice_in_dim(block, 0, width, axis=dim), axis, backward)
        block = jnp.concatenate([low, block, high], axis=dim)
    return block


def from_behind(block, axis, distance):
    devices = range(lax.axis_size(axis))
    route = [(i - distance, i) for i in devices if i - distance in devices]
    return lax.ppermute(block, axis, route)


def contract_rows(left, right):
    return lax.dot_general(
        left, right, (((0,), (0,)), ((), ())), preferred_element_type=jnp.float32
    )


def mm(a, b):
    return jnp.dot(a, b, precision=HIGH, preferred_element_type=jnp.float32)


def inverse_kernel(a_ref, inv_ref, work):
    size = a_ref.shape[0]
    work[...] = a_ref[...]
    rows = lax.broadcasted_iota(jnp.int32, (size, size), 0)
    lanes = lax.broadcasted_iota(jnp.int32, (size, size), 1)
    inv_ref[...] = jnp.where(rows == lanes, 1.0, 0.0).astype(jnp.float32)
    lane = lax.broadcasted_iota(jnp.int32, (1, size), 1)
    sub = lax.broadcasted_iota(jnp.int32, (size, 1), 0)

    def step(k, carry):
        row = work[pl.ds(k, 1), :]
        pivot = jnp.sum(jnp.where(lane == k, row, 0.0), axis=1, keepdims=True)
        scale = lax.rsqrt(pivot)
        whole = work[...]
        column = jnp.sum(jnp.where(lanes == k, whole, 0.0), axis=1, keepdims=True)
        below = jnp.where(sub > k, column * scale, 0.0)
        tail = jnp.where(lane > k, row * scale, 0.0)
        work[...] = whole - below * tail
        lead = inv_ref[pl.ds(k, 1), :] * scale
        current = inv_ref[...]
        inv_ref[...] = jnp.where(rows == k, lead, current - below * lead)
        return carry

    lax.fori_loop(0, size, step, 0)


def block_inverse(block):
    size = block.shape[0]
    return pl.pallas_call(
        inverse_kernel,
        out_shape=jax.ShapeDtypeStruct((size, size), jnp.float32),
        in_specs=[pl.BlockSpec(memory_space=pltpu.VMEM)],
        out_specs=pl.BlockSpec(memory_space=pltpu.VMEM),
        scratch_shapes=[pltpu.VMEM((size, size), jnp.float32)],
        cost_estimate=pl.CostEstimate(flops=4 * size ** 3, bytes_accessed=8 * size * size, transcendentals=size),
    )(block)


def factor(precision, rhs):
    order = precision.shape[0]
    extra = jnp.concatenate([rhs[None], jnp.zeros((7, order), jnp.float32)])
    trailing = jnp.concatenate([precision, extra])
    inverses, panels, forward = [], [], []
    for k in range(order // BLOCK):
        inverse = block_inverse(trailing[:BLOCK, :BLOCK])
        inverses.append(inverse)
        full = mm(trailing[BLOCK:, :BLOCK], inverse.T)
        forward.append(full[-8])
        panel = full[:-8]
        if panel.shape[0]:
            panels.append(panel)
            trailing = trailing[BLOCK:, BLOCK:] - mm(full, panel.T)
    return inverses, panels, forward


def backward(inverses, panels, forward, noise):
    count = len(inverses)
    solved = jnp.zeros((count * BLOCK,), jnp.float32)
    for k in reversed(range(count)):
        value = forward[k] + noise[k * BLOCK : (k + 1) * BLOCK]
        if k < count - 1:
            value = value - mm(panels[k].T, solved[(k + 1) * BLOCK :])
        solved = solved.at[k * BLOCK : (k + 1) * BLOCK].set(mm(inverses[k].T, value))
    return solved


def pair_gather(block, axis, dim):
    if lax.axis_size(axis) != 2:
        return lax.all_gather(block, axis, axis=dim, tiled=True)
    other = lax.ppermute(block, axis, [(0, 1), (1, 0)])
    first = lax.axis_index(axis) == 0
    return jnp.concatenate(
        [jnp.where(first, block, other), jnp.where(first, other, block)], axis=dim
    )


def pair_sum(block, axis):
    if lax.axis_size(axis) != 2:
        return lax.psum(block, axis)
    return block + lax.ppermute(block, axis, [(0, 1), (1, 0)])


def halving_sum(data, axis, late):
    count = lax.axis_size(axis)
    index = lax.axis_index(axis)
    bits = [1 << b for b in range(count.bit_length() - 1)]
    for bit in bits:
        route = [(i, i ^ bit) for i in range(count)]
        half = data.shape[0] // 2
        upper = (index & bit) != 0
        send = jnp.where(upper, data[:half], data[half:])
        keep = jnp.where(upper, data[half:], data[:half])
        data = keep + lax.ppermute(send, axis, route)
    data = jnp.concatenate([data, late])
    for bit in reversed(bits):
        route = [(i, i ^ bit) for i in range(count)]
        upper = (index & bit) != 0
        other = lax.ppermute(data, axis, route)
        data = jnp.concatenate(
            [jnp.where(upper, other, data), jnp.where(upper, data, other)]
        )
    return data.reshape(count, -1, data.shape[-1])


def one_hot(ids, size):
    return (ids[:, None] == lax.broadcasted_iota(jnp.int32, (1, size), 1)).astype(jnp.bfloat16)


def split_parts(values):
    high = lax.reduce_precision(values, exponent_bits=8, mantissa_bits=7)
    rest = values - high
    middle = lax.reduce_precision(rest, exponent_bits=8, mantissa_bits=7)
    low = rest - middle
    return jnp.stack([high, middle, low], axis=1).astype(jnp.bfloat16)


def take_rows(table, ids):
    parts = jnp.dot(one_hot(ids, table.shape[0]), split_parts(table), preferred_element_type=jnp.float32)
    return parts[:, 0] + (parts[:, 1] + parts[:, 2])


def segment_total(values, ids, size):
    parts = contract_rows(one_hot(ids, size), split_parts(values))
    return parts[:, 0] + (parts[:, 1] + parts[:, 2])


def local(design, tract_id, outcome, omega, effects_old, normal_coef, normal_tract):
    columns = design.shape[1]
    tract_dev = effects_old.shape[0]
    kappa = outcome.astype(jnp.float32) - 0.5
    window = extended(effects_old, (("rows", 0),), tract_dev)
    local_id = tract_id - (lax.axis_index("rows") - 1) * tract_dev
    effect_row = take_rows(window, local_id)
    resid = (kappa - omega * effect_row).astype(jnp.bfloat16)
    core = lax.axis_index("cov")
    offset = core * columns
    half = columns // 2
    weighted = (omega[:, None] * design).astype(jnp.bfloat16)
    whole = pair_gather(design, "cov", 1)
    whole_w = (omega[:, None] * whole).astype(jnp.bfloat16)
    own_gram = contract_rows(design, weighted)
    own_sym = own_gram + own_gram.T
    first, second = whole[:, :columns], whole[:, columns:]
    first_w, second_w = whole_w[:, :columns], whole_w[:, columns:]
    cols = lax.dynamic_slice_in_dim(first, core * half, half, axis=1)
    cols_w = lax.dynamic_slice_in_dim(first_w, core * half, half, axis=1)
    cross = contract_rows(second, cols_w) + contract_rows(cols, second_w).T
    rhs_block = contract_rows(resid, design)
    weight_sums = segment_total(omega, local_id, 3 * tract_dev)
    sides = jnp.concatenate([own_sym, cross], axis=1)
    packed = jnp.concatenate(
        [sides[:, j * BLOCK : (j + 1) * BLOCK] for j in range(sides.shape[1] // BLOCK)]
    )
    packed_rows = packed.shape[0]
    extra = columns // BLOCK
    count = lax.axis_size("rows")
    unit = 8 * count
    total = -(-packed_rows // unit) * unit
    if total > packed_rows:
        packed = jnp.concatenate([packed, jnp.zeros((total - packed_rows, BLOCK), jnp.float32)])
    late_rows = -(-extra // 8) * 8
    late = jnp.concatenate(
        [rhs_block.reshape(-1, BLOCK), jnp.zeros((late_rows - extra, BLOCK), jnp.float32)]
    ) + 0.0 * weight_sums[0]
    gathered = halving_sum(packed, "rows", late)
    chunk = total // count
    summed = gathered[:, :chunk].reshape(total, BLOCK)
    rhs_own = jnp.sum(gathered[:, chunk : chunk + extra], axis=0)
    tail = jnp.concatenate([rhs_own, normal_coef.reshape(-1, BLOCK)])
    both = pair_gather(jnp.concatenate([summed[:packed_rows], tail])[None], "cov", 0)
    rhs = both[:, packed_rows : packed_rows + extra].reshape(-1)
    noise = both[:, packed_rows + extra :].reshape(-1)
    strips = both[:, :packed_rows].reshape(2, -1, columns, BLOCK)
    per = columns // BLOCK
    order = 2 * columns
    sym = jnp.concatenate(
        [
            jnp.concatenate([strips[0, t] for t in range(per)] + [jnp.zeros((columns, columns), jnp.float32)], axis=1),
            jnp.concatenate(
                [strips[0, per + t] for t in range(half // BLOCK)]
                + [strips[1, per + t] for t in range(half // BLOCK)]
                + [strips[1, t] for t in range(per)],
                axis=1,
            ),
        ]
    )
    precision = 0.5 * sym + prior_precision * jnp.eye(order, dtype=jnp.float32)
    inverses, panels, forward = factor(precision, rhs)
    beta = backward(inverses, panels, forward, noise)
    beta_b = beta.astype(jnp.bfloat16)
    beta_own = lax.dynamic_slice_in_dim(beta, offset, columns)
    own_coef = lax.dynamic_slice_in_dim(beta_b, offset, columns)
    partial_eta = jnp.dot(design, own_coef, preferred_element_type=jnp.float32)
    eta = pair_sum(partial_eta, "cov")
    contrib = kappa - omega * eta
    resid_sums = segment_total(contrib, local_id, 3 * tract_dev)
    from_above = from_behind((weight_sums[:tract_dev], resid_sums[:tract_dev]), "rows", -1)
    from_below = from_behind((weight_sums[2 * tract_dev :], resid_sums[2 * tract_dev :]), "rows", 1)
    weight_total = weight_sums[tract_dev : 2 * tract_dev] + from_above[0] + from_below[0]
    resid_total = resid_sums[tract_dev : 2 * tract_dev] + from_above[1] + from_below[1]
    prec = tract_precision + weight_total
    effects = resid_total / prec + normal_tract * lax.rsqrt(prec)
    return (beta_own, effects)


def solution(mesh):
    placed = (P("rows", "cov"), P("rows"), P("rows"), P("rows"), P("rows"), P("cov"), P("rows"))
    return jax.shard_map(
        local, mesh=mesh, in_specs=placed, out_specs=(P("cov"), P("rows")), check_vma=False
    )
```
